32 devices in a mesh: seq: 4 (over x, core), dp: 8 (over z, y).
Axes of the slice: x: 2, y: 2, z: 4, core: 2. Of those that a mesh axis runs over, the one named last changes fastest.
Arguments:
- tokens: bfloat16 [8, 2048, 768], P('dp', 'seq'), may hold values from -6 to 6
- prior_logits: float32 [8, 2048, 12], P('dp', 'seq'), may hold values from -6 to 6
- routes: int32 [8, 2048, 2], P('dp', 'seq'), may hold values from 0 to 11, all different within a row; in each aligned block of 2048 rows (0 to 2047, 2048 to 4095, ..., all dimensions but the last counted through in order) at most 512 rows name the same one
- cotangent: bfloat16 [8, 2048, 768], P('dp', 'seq'), may hold values from -6 to 6
- masters: float32 [416, 768, 128], P(('seq', 'dp'))
- owner: int32 [4, 102], P('seq'), may hold values from 0 to 103, as said below
- stat_left: float32 [416, 768, 768], P(('seq', 'dp'))
- stat_right: float32 [416, 128, 128], P(('seq', 'dp'))
- root_left: float32 [416, 768, 768], P(('seq', 'dp'))
- root_right: float32 [416, 128, 128], P(('seq', 'dp'))
- gain_attn: float32 [768], replicated, may hold values from 0.5 to 1.5
- gain_moe: float32 [768], replicated, may hold values from 0.5 to 1.5
- router: float32 [768, 12], replicated, may hold values from -0.21875 to 0.21875
- router_prior: float32 [12, 12], replicated, may hold values from -1.75 to 1.75
- const_mix: float32 [2, 768, 2], replicated, may hold values from -0.21875 to 0.21875
- const_value: float32 [2, 768], replicated, may hold values from -6 to 6
- adam_first: float32 [15504], replicated
- adam_second: float32 [15504], replicated
Outputs:
- block_out: bfloat16 [8, 2048, 768], P('dp', 'seq')
- input_grad: float32 [8, 2048, 768], P('dp', 'seq')
- prior_grad: float32 [8, 2048, 12], P('dp', 'seq')
- block_grads: float32 [416, 768, 128], P(('seq', 'dp'))
- new_masters: float32 [416, 768, 128], P(('seq', 'dp'))
- new_left: float32 [416, 768, 768], P(('seq', 'dp'))
- new_right: float32 [416, 128, 128], P(('seq', 'dp'))
- small_grads: float32 [15504], replicated
- new_small: float32 [15504], replicated
- new_first: float32 [15504], replicated
- new_second: float32 [15504], replicated
The draws below stay inside these ranges and needn't reach their ends.
Inputs may be any that keep to these rules, and one draw needn't show every extreme that they name: In each sequence no route is named by more than 512 choices; a token's two routes differ. `owner`: the 102 entries of a row are distinct slots.
All inputs are finite; a program needn't handle non-finite values.
Results may differ from the reference program's by a relative error of at most 0.02.
Values may be sent and summed in bfloat16 or wider, within the bound.
No kernel may reach another device: no remote copies, remote signals or barrier semaphores. Data moves between devices by JAX's collectives and lax.ppermute only.
A program may use at most 320 MiB of HBM per device.

```python
import math
import jax
import jax.numpy as jnp
import numpy as np
from jax import lax

D = 768
HEADS = 12
HEAD = 64
FF = 2048
EXPERTS = 8
ROUTES = 12
BW = 128
STEP = 4
LENGTH = 2048
BATCH = 8
CAP = 512
ROW_BLOCKS = 102
ROW_SLOTS = 104
SLOTS = 416
SMALL = 15504
N_SEQ = 4


def owner_table(key):

    def one_row(row_key):
        first_key, second_key = jax.random.split(row_key)
        middle = jax.random.permutation(first_key, ROW_SLOTS - 2)[:ROW_BLOCKS - 2].astype(jnp.int32) + 1
        ends = jnp.array([0, ROW_SLOTS - 1], dtype=jnp.int32)
        return jax.random.permutation(second_key, jnp.concatenate([middle, ends]))
    return jax.vmap(one_row)(jax.random.split(jax.random.fold_in(key, 11), N_SEQ))


def draw_owner(key, part):
    return owner_table(key)


def draw_masters(key, part):
    table = owner_table(key)
    base = jax.random.normal(jax.random.fold_in(key, 3), (SLOTS, D, BW), jnp.float32) * D ** (-0.5)
    attn_row = 4 * D // (BW * N_SEQ)
    col_start = (jnp.arange(N_SEQ)[:, None] * attn_row + jnp.arange(attn_row)[None, :]) * BW
    out_scale = jnp.where(col_start >= 3 * D, 8.0, 1.0).astype(jnp.float32)
    slot_ids = jnp.arange(N_SEQ, dtype=jnp.int32)[:, None] * ROW_SLOTS + table[:, :attn_row]
    scale = jnp.ones((SLOTS,), jnp.float32).at[slot_ids.reshape(-1)].set(out_scale.reshape(-1))
    return base * scale[:, None, None]


def symmetric_draw(key, count, size, diag_low, diag_high, spread):
    diag_key, noise_key = jax.random.split(key)
    diagonal = jnp.exp(jax.random.uniform(diag_key, (count, size), jnp.float32, math.log(diag_low), math.log(diag_high)))
    noise = jax.random.normal(noise_key, (count, size, size), jnp.float32) * (spread / math.sqrt(size))
    noise = (noise + jnp.swapaxes(noise, 1, 2)) * 0.5
    return noise + diagonal[:, :, None] * jnp.eye(size, dtype=jnp.float32)[None]


def draw_stat_left(key, part):
    factor = float(BW * BATCH * LENGTH)
    return symmetric_draw(jax.random.fold_in(key, 21), SLOTS, D, 0.1, 1.0, 0.1) * factor


def draw_stat_right(key, part):
    factor = float(D * BATCH * LENGTH)
    return symmetric_draw(jax.random.fold_in(key, 22), SLOTS, BW, 0.1, 1.0, 0.1) * factor


def draw_root_left(key, part):
    return symmetric_draw(jax.random.fold_in(key, 23), SLOTS, D, 0.05, 0.3, 0.1)


def draw_root_right(key, part):
    return symmetric_draw(jax.random.fold_in(key, 24), SLOTS, BW, 0.05, 0.3, 0.1)


def draw_adam_first(key, part):
    factor = 0.1 * math.sqrt(float(BATCH * LENGTH))
    values = jax.random.normal(jax.random.fold_in(key, 31), (SMALL,), jnp.float32)
    return jnp.clip(values, -6.0, 6.0) * factor


def draw_adam_second(key, part):
    factor = float(BATCH * LENGTH)
    spread = jax.random.uniform(jax.random.fold_in(key, 32), (SMALL,), jnp.float32, math.log(0.0005), math.log(0.05))
    return jnp.exp(spread) * factor


def block_levels(rng, dims, cuts, low, largest):
    factor_of = 1.0
    for position, shards_of in cuts:
        heights = jax.random.uniform(jax.random.fold_in(jax.random.fold_in(rng, 6), position), (shards_of,), jnp.float32, low / len(cuts), largest / len(cuts))
        factor_of = factor_of * jnp.repeat(jnp.exp(heights), dims[position] // shards_of).reshape((-1,) + (1,) * (len(dims) - 1 - position))
    return factor_of


def routed_block(own_key, own, number, rows, count, top, limit, lean):
    sequence = jax.random.permutation(own_key, count)
    crowded, common = load_shares(count, rows * top, limit, lean, True), load_shares(count, rows * top, limit, lean, False)
    places = jnp.arange(count)

    def named(lengths, turn):
        used = int((lengths > 0).sum())
        fixed = max(1, used // 4)
        shifted = fixed + (places - fixed + turn * (used - fixed)) % max(1, count - fixed)
        return jnp.zeros((count,), jnp.int32).at[sequence[jnp.where(places < fixed, places, shifted)]].set(jnp.asarray(lengths, jnp.int32))

    lengths = jnp.where(number % 4 == 0, named(crowded, number // 4), named(common, number - number // 4 - 1))
    mixed = jax.random.permutation(jax.random.fold_in(own, 3), count)
    source_of, receiver = mixed[0:count // 2 * 2:2], mixed[1:count // 2 * 2:2]
    slack = jnp.minimum(lengths[source_of] - 1, limit - lengths[receiver]) // 2
    slack = jnp.where((source_of == sequence[0]) | (receiver == sequence[0]) | (lengths[receiver] == 0), 0, jnp.maximum(slack, 0))
    shifted = jax.random.randint(jax.random.fold_in(own, 4), (count // 2,), 0, 1 << 20) % (slack + 1)
    lengths = lengths.at[source_of].add(-shifted).at[receiver].add(shifted)
    labels = jnp.searchsorted(jnp.cumsum(lengths), jnp.arange(rows * top), side="right").astype(jnp.int32)
    grid = labels.reshape(top, rows).T
    grid = grid[jax.random.permutation(jax.random.fold_in(own, 1), rows)]
    turn = jax.random.randint(jax.random.fold_in(own, 2), (rows, 1), 0, top)
    return jnp.take_along_axis(grid, (jnp.arange(top)[None, :] + turn) % top, axis=1)


def load_shares(count, total, most, skew, full):
    weights = [(1 << 20) // math.isqrt(standing ** skew) + 1 for standing in range(1, count + 1)]
    largest = most if full else min(most, max(-(-total // count), total * weights[0] // sum(weights)))
    least = 1 if total - largest >= count - 1 else 0
    given, spare = [largest] + [least] * (count - 1), total - largest - least * (count - 1)
    while spare > 0:
        candidates = [i for i in range(1, count) if given[i] < largest] or [i for i in range(1, count) if given[i] < most]
        pool, budget = sum([weights[i] for i in candidates]), spare
        for i in candidates:
            more = min(most - given[i], max(1, budget * weights[i] // pool), spare)
            given[i] = given[i] + more
            spare = spare - more
    return np.array(given)


def centred(rng, extent, deviation, limit, cuts=(), held_as=jnp.bfloat16):
    values = jax.random.normal(rng, extent, jnp.float32) * deviation
    if len(cuts) > 0:
        values = block_levels(rng, extent, cuts, -0.22, 0.18) * values
    return jnp.clip(values, min=-limit, max=limit).astype(held_as)


def setup_inputs(seed: int = 0) -> dict:
    seeds = jax.random.split(jax.random.key(seed), 19)
    tokens = centred(seeds[0], (BATCH, LENGTH, D), 1.0, 6.0, ((0, 8), (1, 4)))
    prior_logits = centred(seeds[1], (BATCH, LENGTH, ROUTES), 1.0, 6.0, ((0, 8), (1, 4)), jnp.float32)
    routes_keys = jax.random.split(jax.random.fold_in(seeds[2], 1), BATCH * LENGTH // LENGTH)
    routes_turns = jax.random.permutation(jax.random.fold_in(seeds[2], 3), BATCH * LENGTH // LENGTH)
    routes = jax.vmap(lambda own, number: routed_block(jax.random.fold_in(seeds[2], 2), own, number, LENGTH, ROUTES, 2, CAP, 1))(routes_keys, routes_turns).reshape((BATCH, LENGTH, 2))
    cotangent = centred(seeds[3], (BATCH, LENGTH, D), 1.0, 6.0, ((0, 8), (1, 4)))
    masters = draw_masters(jax.random.fold_in(seeds[18], 71), 0)
    owner = draw_owner(jax.random.fold_in(seeds[18], 71), 0)
    stat_left = draw_stat_left(jax.random.fold_in(seeds[18], 71), 0)
    stat_right = draw_stat_right(jax.random.fold_in(seeds[18], 71), 0)
    root_left = draw_root_left(jax.random.fold_in(seeds[18], 71), 0)
    root_right = draw_root_right(jax.random.fold_in(seeds[18], 71), 0)
    gain_attn = jnp.clip(1.0 + 0.1 * jax.random.normal(seeds[10], (D,), jnp.float32), 0.5, 1.5)
    gain_moe = jnp.clip(1.0 + 0.1 * jax.random.normal(seeds[11], (D,), jnp.float32), 0.5, 1.5)
    router = centred(seeds[12], (D, ROUTES), D ** -0.5, 0.21875, (), jnp.float32)
    router_prior = centred(seeds[13], (ROUTES, ROUTES), ROUTES ** -0.5, 1.75, (), jnp.float32)
    const_mix = centred(seeds[14], (2, D, 2), D ** -0.5, 0.21875, (), jnp.float32)
    const_value = centred(seeds[15], (2, D), 1.0, 6.0, (), jnp.float32)
    adam_first = draw_adam_first(jax.random.fold_in(seeds[18], 71), 0)
    adam_second = draw_adam_second(jax.random.fold_in(seeds[18], 71), 0)
    return {"tokens": tokens, "prior_logits": prior_logits, "routes": routes, "cotangent": cotangent, "masters": masters, "owner": owner, "stat_left": stat_left, "stat_right": stat_right, "root_left": root_left, "root_right": root_right, "gain_attn": gain_attn, "gain_moe": gain_moe, "router": router, "router_prior": router_prior, "const_mix": const_mix, "const_value": const_value, "adam_first": adam_first, "adam_second": adam_second}


norm_eps = 1e-06
rope_base = 10000.0
stat_decay = 0.5
shampoo_rate = 0.1
adam_rate = 0.01
first_decay = 0.9
second_decay = 0.999
adam_eps = 1e-08

@jax.custom_vjp
def low(v):
    return lax.optimization_barrier(v.astype(jnp.bfloat16)).astype(jnp.float32)

@jax.custom_vjp
def low_back(v):
    return v

def low_keep(v):
    return (low(v), None)

def low_pass(kept, grad):
    return (grad,)

def back_keep(v):
    return (v, None)

def back_low(kept, grad):
    return (low(grad),)
low.defvjp(low_keep, low_pass)
low_back.defvjp(back_keep, back_low)

def rms_scale(values, gain):
    return values * lax.rsqrt(lax.optimization_barrier(jnp.mean(values * values, axis=-1, keepdims=True)) + norm_eps) * gain

def rotate(values, positions):
    half_dim = values.shape[-1] // 2
    freq = rope_base ** (-(jnp.arange(half_dim, dtype=jnp.float32) * 2.0 / values.shape[-1]))
    angles = positions[:, None].astype(jnp.float32) * freq[None, :]
    cosine = jnp.cos(angles)[:, None, :]
    sine = jnp.sin(angles)[:, None, :]
    first_half = values[..., :half_dim]
    second_half = values[..., half_dim:]
    return jnp.concatenate([first_half * cosine - second_half * sine, second_half * cosine + first_half * sine], axis=-1)

def group_slots(route_flat, capacity, expert_count):
    pair_total = route_flat.shape[0]
    order = jnp.argsort(route_flat * pair_total + jnp.arange(pair_total, dtype=jnp.int32)).astype(jnp.int32)
    counts = lax.optimization_barrier(jnp.sum((route_flat[None, :] == jnp.arange(expert_count, dtype=jnp.int32)[:, None]).astype(jnp.int32), axis=1))
    starts = (jnp.cumsum(counts) - counts).astype(jnp.int32)
    padded = jnp.concatenate([order, jnp.zeros((capacity,), jnp.int32)])
    pair_ids = jax.vmap(lambda begin: lax.dynamic_slice_in_dim(padded, begin, capacity))(starts)
    valid = jnp.arange(capacity, dtype=jnp.int32)[None, :] < counts[:, None]
    return (pair_ids, valid)

def local_experts(hidden, picked, route_rows, const_mix, const_value):
    highest = lax.Precision.HIGHEST
    copy_weight = lax.optimization_barrier(jnp.sum(picked * (route_rows == EXPERTS + 1), axis=1))
    mixing = jax.nn.softmax(jnp.einsum('td,cdm->ctm', hidden, const_mix, precision=highest), axis=-1)
    result = copy_weight[:, None] * hidden
    for const_id in range(2):
        weight = lax.optimization_barrier(jnp.sum(picked * (route_rows == EXPERTS + 2 + const_id), axis=1))
        result = result + weight[:, None] * (mixing[const_id][:, 0:1] * hidden + mixing[const_id][:, 1:2] * const_value[const_id][None, :])
    return result

def local_part(route_rows, hidden, prior_rows, router, router_prior, const_mix, const_value):
    highest = lax.Precision.HIGHEST
    logits = jnp.dot(hidden, router, precision=highest) + jnp.dot(prior_rows, router_prior, precision=highest)
    chosen = jnp.take_along_axis(logits, route_rows, axis=1)
    picked = jax.nn.softmax(chosen, axis=-1)
    return (local_experts(hidden, picked, route_rows, const_mix, const_value), picked)

def sequence_forward(param_set, seq_tokens, seq_prior, seq_routes):
    attn_w, expert_w, gain_attn, gain_moe, router, router_prior, const_mix, const_value = param_set
    highest = lax.Precision.HIGHEST
    rows = seq_tokens.shape[0]
    positions = jnp.arange(rows, dtype=jnp.int32)
    normed = low(rms_scale(seq_tokens, gain_attn))
    projected = jnp.dot(normed, attn_w[:, :3 * D], precision=highest)
    queries = low(rotate(low_back(projected[:, :D]).reshape(rows, HEADS, HEAD), positions))
    keys = low(rotate(low_back(projected[:, D:2 * D]).reshape(rows, HEADS, HEAD), positions))
    values = low(low_back(projected[:, 2 * D:])).reshape(rows, HEADS, HEAD)
    scores = low_back(jnp.einsum('qhd,khd->hqk', queries, keys, precision=highest) * HEAD ** (-0.5))
    causal = positions[None, :] <= positions[:, None]
    scores = jnp.where(causal[None], scores, -1e+30)
    probs = low(jax.nn.softmax(scores, axis=-1))
    context = low(low_back(jnp.einsum('hqk,khd->qhd', probs, values, precision=highest).reshape(rows, D)))
    attn_out = low_back(jnp.dot(context, attn_w[:, 3 * D:], precision=highest))
    mid = seq_tokens + attn_out
    hidden = rms_scale(mid, gain_moe)
    hidden_low = low(hidden)
    local_out, picked = local_part(seq_routes, hidden, seq_prior, router, router_prior, const_mix, const_value)
    gate_low = low(picked)
    pair_ids, valid = group_slots(seq_routes.reshape(-1), CAP, EXPERTS)
    token_ids = pair_ids // 2
    slot_gates = jnp.where(valid, gate_low.reshape(-1)[pair_ids], 0.0)
    expert_in = hidden_low[token_ids]
    gate_act = low_back(jnp.einsum('ecd,edf->ecf', expert_in, expert_w[:, 0], precision=highest))
    up_act = low_back(jnp.einsum('ecd,edf->ecf', expert_in, expert_w[:, 1], precision=highest))
    act = low(jax.nn.silu(gate_act) * up_act)
    expert_out = low_back(jnp.einsum('ecf,edf->ecd', act, expert_w[:, 2], precision=highest))
    weighted = expert_out * slot_gates[..., None]
    ffn_out = low_back(jnp.zeros((rows, D), jnp.float32).at[token_ids.reshape(-1)].add(weighted.reshape(-1, D)))
    return mid + ffn_out + local_out

def pack_small(gain_attn, gain_moe, router, router_prior, const_mix, const_value):
    return jnp.concatenate([gain_attn, gain_moe, router.reshape(-1), router_prior.reshape(-1), const_mix.reshape(-1), const_value.reshape(-1)])

def adam_update(params_flat, grads_flat, first, second):
    new_first = first_decay * first + (1.0 - first_decay) * grads_flat
    new_second = second_decay * second + (1.0 - second_decay) * grads_flat * grads_flat
    corrected_first = new_first / (1.0 - first_decay ** STEP)
    corrected_second = new_second / (1.0 - second_decay ** STEP)
    return (params_flat - adam_rate * corrected_first / (jnp.sqrt(corrected_second) + adam_eps), new_first, new_second)

def shampoo_update(masters, grads, stat_left, stat_right, root_left, root_right):
    highest = lax.Precision.HIGHEST
    new_left = stat_decay * stat_left + (1.0 - stat_decay) * jnp.einsum('sik,sjk->sij', grads, grads, precision=highest)
    new_right = stat_decay * stat_right + (1.0 - stat_decay) * jnp.einsum('ski,skj->sij', grads, grads, precision=highest)
    update = jnp.einsum('sij,sjk->sik', root_left, grads, precision=highest)
    update = jnp.einsum('sik,skl->sil', update, root_right, precision=highest)
    return (masters - shampoo_rate * update, new_left, new_right)

def reference(tokens, prior_logits, routes, cotangent, masters, owner, stat_left, stat_right, root_left, root_right, gain_attn, gain_moe, router, router_prior, const_mix, const_value, adam_first, adam_second):
    row_slots = masters.shape[0] // N_SEQ
    attn_row = 4 * D // (BW * N_SEQ)
    nj_count = FF // (N_SEQ * BW)
    slab = masters.reshape(N_SEQ, row_slots, D, BW)
    picked_blocks = jax.vmap(lambda one_row, slot_ids: one_row[slot_ids])(slab, owner)
    weights_low = low(picked_blocks)
    attn_w = weights_low[:, :attn_row].transpose(2, 0, 1, 3).reshape(D, 4 * D)
    expert_w = weights_low[:, attn_row:].reshape(N_SEQ, EXPERTS, 3, nj_count, D, BW).transpose(1, 2, 4, 0, 3, 5).reshape(EXPERTS, 3, D, FF)
    param_set = (attn_w, expert_w, gain_attn, gain_moe, router, router_prior, const_mix, const_value)
    zero_grads = jax.tree.map(jnp.zeros_like, param_set)

    def one_sequence(total, inputs):
        seq_tokens, seq_prior, seq_routes, seq_cot = inputs
        result, back = jax.vjp(lambda params_in, tok_rows, prior_rows: sequence_forward(params_in, tok_rows, prior_rows, seq_routes), param_set, seq_tokens, seq_prior)
        param_grad, tok_grad, prior_grad_one = back(seq_cot)
        total = jax.tree.map(lambda acc_grad, new_grad: acc_grad + new_grad, total, param_grad)
        return (total, (result.astype(jnp.bfloat16), tok_grad, prior_grad_one))
    grads, (block_out, input_grad, prior_grad) = lax.scan(one_sequence, zero_grads, (tokens.astype(jnp.float32), prior_logits, routes, cotangent.astype(jnp.float32)))
    attn_blocks = grads[0].reshape(D, N_SEQ, attn_row, BW).transpose(1, 2, 0, 3)
    expert_blocks = grads[1].reshape(EXPERTS, 3, D, N_SEQ, nj_count, BW).transpose(3, 0, 1, 4, 2, 5).reshape(N_SEQ, -1, D, BW)
    row_grads = jnp.concatenate([attn_blocks, expert_blocks], axis=1)
    slot_ids = (jnp.arange(N_SEQ, dtype=jnp.int32)[:, None] * row_slots + owner).reshape(-1)
    block_grads = jnp.zeros_like(masters).at[slot_ids].set(row_grads.reshape(-1, D, BW))
    new_masters, new_left, new_right = shampoo_update(masters, block_grads, stat_left, stat_right, root_left, root_right)
    small_grads = pack_small(grads[2], grads[3], grads[4], grads[5], grads[6], grads[7])
    small_now = pack_small(gain_attn, gain_moe, router, router_prior, const_mix, const_value)
    new_small, new_first, new_second = adam_update(small_now, small_grads, adam_first, adam_second)
    return (block_out, input_grad, prior_grad, block_grads, new_masters, new_left, new_right, small_grads, new_small, new_first, new_second)
```

```python
from functools import partial

import numpy as np

import jax
import jax.numpy as jnp
from jax import lax
from jax.sharding import PartitionSpec as P

D = 768
HEADS = 12
HEAD = 64
EXPERTS = 8
BW = 128
STEP = 4


norm_eps = 1e-06
rope_base = 10000.0
stat_decay = 0.5
shampoo_rate = 0.1
adam_rate = 0.01
first_decay = 0.9
second_decay = 0.999
adam_eps = 1e-08


def rms_scale(values, gain):
    return values * lax.rsqrt(jnp.mean(values * values, axis=-1, keepdims=True) + norm_eps) * gain


def rotate(values, positions):
    half_dim = values.shape[-1] // 2
    freq = rope_base ** (-(jnp.arange(half_dim, dtype=jnp.float32) * 2.0 / values.shape[-1]))
    angles = positions[:, None].astype(jnp.float32) * freq[None, :]
    cosine = jnp.cos(angles)[:, None, :]
    sine = jnp.sin(angles)[:, None, :]
    first_half = values[..., :half_dim]
    second_half = values[..., half_dim:]
    return jnp.concatenate(
        [first_half * cosine - second_half * sine, second_half * cosine + first_half * sine],
        axis=-1,
    )


def group_slots(route_flat, capacity, expert_count):
    pair_total = route_flat.shape[0]
    order = jnp.argsort(route_flat * pair_total + jnp.arange(pair_total, dtype=jnp.int32))
    counts = jnp.sum(
        (route_flat[None, :] == jnp.arange(expert_count, dtype=jnp.int32)[:, None]).astype(
            jnp.int32
        ),
        axis=1,
    )
    starts = jnp.cumsum(counts) - counts
    padded = jnp.concatenate([order, jnp.zeros((capacity,), jnp.int32)])
    pair_ids = jax.vmap(lambda begin: lax.dynamic_slice_in_dim(padded, begin, capacity))(starts)
    valid = jnp.arange(capacity, dtype=jnp.int32)[None, :] < counts[:, None]
    return (pair_ids, valid)


def local_experts(hidden, picked, route_rows, const_mix, const_value):
    highest = lax.Precision.HIGHEST
    copy_weight = jnp.sum(picked * (route_rows == EXPERTS + 1), axis=1)
    mixing = jax.nn.softmax(
        jnp.einsum("td,cdm->ctm", hidden, const_mix, precision=highest), axis=-1
    )
    result = copy_weight[:, None] * hidden
    for const_id in range(2):
        weight = jnp.sum(picked * (route_rows == EXPERTS + 2 + const_id), axis=1)
        result = result + weight[:, None] * (
            mixing[const_id][:, 0:1] * hidden
            + mixing[const_id][:, 1:2] * const_value[const_id][None, :]
        )
    return result


def local_part(route_rows, hidden, prior_rows, router, router_prior, const_mix, const_value):
    highest = lax.Precision.HIGHEST
    logits = jnp.dot(hidden, router, precision=highest) + jnp.dot(
        prior_rows, router_prior, precision=highest
    )
    chosen = jnp.take_along_axis(logits, route_rows, axis=1)
    picked = jax.nn.softmax(chosen, axis=-1)
    return (local_experts(hidden, picked, route_rows, const_mix, const_value), picked)


def arrange_experts(pieces):
    nj_count = pieces.shape[0] // (3 * EXPERTS)
    shaped = pieces.reshape(EXPERTS, 3, nj_count, D, BW)
    return shaped.transpose(0, 1, 3, 2, 4).reshape(EXPERTS, 3, D, nj_count * BW)


def add_rows(total, piece, offset):
    current = lax.dynamic_slice_in_dim(total, offset, piece.shape[0], 0)
    return lax.dynamic_update_slice_in_dim(total, current + piece, offset, 0)


def over_blocks(carry, keys_in, values_in, block_len, step_fn):
    count = keys_in.shape[0]
    steps_count = count // block_len

    def scan_step(inner, block_in):
        key_block, value_block, offset = block_in
        return (step_fn(inner, key_block, value_block, offset), None)

    offsets = jnp.arange(steps_count, dtype=jnp.int32) * block_len
    carry, _ = lax.scan(
        scan_step,
        carry,
        (
            keys_in.reshape(steps_count, block_len, -1),
            values_in.reshape(steps_count, block_len, -1),
            offsets,
        ),
    )
    return carry


def shampoo_update(masters, grads, stat_left, stat_right, root_left, root_right):
    highest = lax.Precision.HIGHEST
    new_left = stat_decay * stat_left + (1.0 - stat_decay) * jnp.einsum(
        "sik,sjk->sij", grads, grads, precision=highest
    )
    new_right = stat_decay * stat_right + (1.0 - stat_decay) * jnp.einsum(
        "ski,skj->sij", grads, grads, precision=highest
    )
    update = jnp.einsum("sij,sjk->sik", root_left, grads, precision=highest)
    update = jnp.einsum("sik,skl->sil", update, root_right, precision=highest)
    return (masters - shampoo_rate * update, new_left, new_right)


def pack_small(gain_attn, gain_moe, router, router_prior, const_mix, const_value):
    return jnp.concatenate(
        [
            gain_attn,
            gain_moe,
            router.reshape(-1),
            router_prior.reshape(-1),
            const_mix.reshape(-1),
            const_value.reshape(-1),
        ]
    )


def adam_update(params_flat, grads_flat, first, second):
    new_first = first_decay * first + (1.0 - first_decay) * grads_flat
    new_second = second_decay * second + (1.0 - second_decay) * grads_flat * grads_flat
    corrected_first = new_first / (1.0 - first_decay**STEP)
    corrected_second = new_second / (1.0 - second_decay**STEP)
    return (
        params_flat - adam_rate * corrected_first / (jnp.sqrt(corrected_second) + adam_eps),
        new_first,
        new_second,
    )


def snake_ring(mesh, axis):
    devs = np.asarray(mesh.devices)
    ax = mesh.axis_names.index(axis)
    count = devs.shape[ax]
    line = [devs[(0,) * ax + (i,) + (0,) * (devs.ndim - ax - 1)] for i in range(count)]
    try:
        coords = [tuple(int(c) for c in d.coords) + (int(d.core_on_chip),) for d in line]
    except Exception:
        return list(range(count))
    vary = [j for j in range(len(coords[0])) if len({c[j] for c in coords}) > 1]
    if len(vary) == 1:
        return sorted(range(count), key=lambda i: coords[i][vary[0]])
    if len(vary) != 2:
        return list(range(count))
    ja, jb = vary
    vals_a = sorted({c[ja] for c in coords})
    vals_b = sorted({c[jb] for c in coords})
    na, nb = len(vals_a), len(vals_b)
    if na * nb != count:
        return list(range(count))
    where = {(vals_a.index(c[ja]), vals_b.index(c[jb])): i for i, c in enumerate(coords)}
    if nb % 2 == 1 and na % 2 == 0:
        where = {(b, a): i for (a, b), i in where.items()}
        na, nb = nb, na
    if nb % 2 == 1 or na < 2:
        return list(range(count))
    cycle = []
    for b in range(nb):
        span = range(1, na) if b % 2 == 0 else range(na - 1, 0, -1)
        cycle += [where[(a, b)] for a in span]
    cycle += [where[(0, b)] for b in range(nb - 1, -1, -1)]
    return cycle


def ring_position(ring, axis):
    pos_of = [0] * len(ring)
    for q, d in enumerate(ring):
        pos_of[d] = q
    return jnp.asarray(pos_of, jnp.int32)[lax.axis_index(axis)]


def ring_gather(x, ring, axis):
    count = len(ring)
    fwd = [(ring[q], ring[(q + 1) % count]) for q in range(count)]
    bwd = [(ring[(q + 1) % count], ring[q]) for q in range(count)]
    half = x.shape[1] // 2
    a, b = x[:, :half], x[:, half:]
    got_a, got_b = [a], [b]
    for _ in range(1, count):
        a = lax.ppermute(a, axis, fwd)
        b = lax.ppermute(b, axis, bwd)
        got_a.append(a)
        got_b.append(b)
    return jnp.stack(got_a), jnp.stack(got_b)


def ring_reduce_scatter(chunks_a, chunks_b, ring, axis):
    count = len(ring)
    fwd = [(ring[q], ring[(q + 1) % count]) for q in range(count)]
    bwd = [(ring[(q + 1) % count], ring[q]) for q in range(count)]
    me = ring_position(ring, axis)
    f32 = jnp.float32
    pick = lambda chunks, q: lax.dynamic_index_in_dim(chunks, q % count, 0, keepdims=False)
    acc_a = pick(chunks_a, me - 1).astype(f32)
    acc_b = pick(chunks_b, me + 1).astype(f32)
    for k in range(1, count):
        acc_a = lax.ppermute(acc_a.astype(jnp.bfloat16), axis, fwd).astype(f32) + pick(
            chunks_a, me - 1 - k
        ).astype(f32)
        acc_b = lax.ppermute(acc_b.astype(jnp.bfloat16), axis, bwd).astype(f32) + pick(
            chunks_b, me + 1 + k
        ).astype(f32)
    return acc_a, acc_b


def body(
    dp_ring,
    tokens,
    prior_logits,
    routes,
    cotangent,
    masters,
    owner,
    stat_left,
    stat_right,
    root_left,
    root_right,
    gain_attn,
    gain_moe,
    router,
    router_prior,
    const_mix,
    const_value,
    adam_first,
    adam_second,
):
    highest = lax.Precision.HIGHEST
    f32 = jnp.float32
    bf16 = jnp.bfloat16
    seq_count = lax.axis_size("seq")
    dp_count = lax.axis_size("dp")
    seq_rank = lax.axis_index("seq")
    dp_rank = lax.axis_index("dp")
    tok_rows = tokens.shape[1]
    group_rows = tok_rows * seq_count
    capacity = group_rows // 4
    n_local = masters.shape[0]
    row_slots = n_local * dp_count
    attn_row = 4 * D // (BW * seq_count)
    nj_count = (owner.shape[1] - attn_row) // (3 * EXPERTS)
    score_scale = HEAD ** (-0.5)
    positions = seq_rank * tok_rows + jnp.arange(tok_rows, dtype=jnp.int32)
    last_query = seq_rank * tok_rows + tok_rows - 1
    me = ring_position(dp_ring, "dp")
    ring_arr = jnp.asarray(dp_ring, jnp.int32)
    pos_of = [0] * len(dp_ring)
    for q, d in enumerate(dp_ring):
        pos_of[d] = q
    pos_arr = jnp.asarray(pos_of, jnp.int32)

    slots_local = masters.astype(bf16)
    got_a, got_b = ring_gather(slots_local, dp_ring, "dp")
    owner_row = owner[0]
    slot_dev = owner_row // n_local
    slot_idx = owner_row % n_local
    expert_dev = slot_dev[attn_row:]
    expert_idx = slot_idx[attn_row:]
    k_a = (me - pos_arr[expert_dev]) % dp_count
    k_b = (pos_arr[expert_dev] - me) % dp_count
    span = jnp.arange(row_slots, dtype=jnp.int32)[None, :]
    pick_a = ((k_a * n_local + expert_idx)[:, None] == span).astype(bf16)
    pick_b = ((k_b * n_local + expert_idx)[:, None] == span).astype(bf16)
    half_rows = got_a.shape[2]
    top = jnp.einsum(
        "bi,irc->brc", pick_a, got_a.reshape(row_slots, half_rows, BW), preferred_element_type=bf16
    )
    bottom = jnp.einsum(
        "bi,irc->brc", pick_b, got_b.reshape(row_slots, half_rows, BW), preferred_element_type=bf16
    )
    expert_blocks = jnp.concatenate([top, bottom], axis=1).reshape(
        EXPERTS, 3, nj_count, D, BW
    )

    local_span = jnp.arange(n_local, dtype=jnp.int32)[None, :]
    attn_sel = (
        (slot_dev[:attn_row] == dp_rank)[:, None] & (slot_idx[:attn_row][:, None] == local_span)
    ).astype(bf16)
    attn_local = jnp.einsum("bi,irc->brc", attn_sel, slots_local, preferred_element_type=bf16)
    attn_rows = lax.psum_scatter(attn_local, "dp", scatter_dimension=1, tiled=True)
    shard_rows = attn_rows.shape[1]
    attn_pieces = lax.all_gather(attn_rows, ("seq", "dp"), axis=0, tiled=True)
    attn_full = (
        attn_pieces.reshape(seq_count, dp_count, attn_row, shard_rows, BW)
        .transpose(1, 3, 0, 2, 4)
        .reshape(D, 4 * D)
    )
    weight_qkv = attn_full[:, : 3 * D]
    weight_out = attn_full[:, 3 * D :]
    x_rows = tokens[0].astype(f32)
    normed = rms_scale(x_rows, gain_attn)
    normed_b = normed.astype(bf16)
    projected = jnp.dot(normed_b, weight_qkv, preferred_element_type=f32)
    queries = rotate(projected[:, :D].reshape(tok_rows, HEADS, HEAD), positions).astype(bf16)
    keys_b = (
        rotate(projected[:, D : 2 * D].reshape(tok_rows, HEADS, HEAD), positions)
        .astype(bf16)
        .reshape(tok_rows, D)
    )
    values_b = projected[:, 2 * D :].astype(bf16)

    def forward_block(carry, key_block, value_block, offset):

        def forward_visit(inner):
            row_max, row_sum, accum = inner
            count = key_block.shape[0]
            key_heads = key_block.reshape(count, HEADS, HEAD)
            scores = (
                jnp.einsum("qhd,khd->hqk", queries, key_heads, preferred_element_type=f32)
                * score_scale
            )
            allowed = (offset + jnp.arange(count, dtype=jnp.int32))[None, :] <= positions[:, None]
            scores = jnp.where(allowed[None], scores, -1e30)
            new_max = jnp.maximum(row_max, jnp.max(scores, axis=-1))
            factor = jnp.exp(row_max - new_max)
            weights = jnp.where(allowed[None], jnp.exp(scores - new_max[..., None]), 0.0)
            row_sum = row_sum * factor + jnp.sum(weights, axis=-1)
            accum = accum * factor[..., None] + jnp.einsum(
                "hqk,khd->hqd",
                weights.astype(bf16),
                value_block.reshape(count, HEADS, HEAD),
                preferred_element_type=f32,
            )
            return (new_max, row_sum, accum)

        return lax.cond(offset <= last_query, forward_visit, lambda inner: inner, carry)

    fold_init = (
        jnp.full((HEADS, tok_rows), -1e30, f32),
        jnp.zeros((HEADS, tok_rows), f32),
        jnp.zeros((HEADS, tok_rows, HEAD), f32),
    )
    piece = (
        lax.all_gather(keys_b, "seq", axis=0, tiled=True),
        lax.all_gather(values_b, "seq", axis=0, tiled=True),
    )
    row_max, row_sum, accum = over_blocks(fold_init, piece[0], piece[1], tok_rows, forward_block)
    context = accum / row_sum[..., None]
    log_total = row_max + jnp.log(row_sum)
    context_b = context.transpose(1, 0, 2).reshape(tok_rows, D).astype(bf16)
    mid_rows = x_rows + jnp.dot(context_b, weight_out, preferred_element_type=f32)
    route_rows = routes[0]
    hidden = rms_scale(mid_rows, gain_moe)
    hidden_b = hidden.astype(bf16)
    (local_out, picked), local_back = jax.vjp(
        partial(local_part, route_rows),
        hidden,
        prior_logits[0],
        router,
        router_prior,
        const_mix,
        const_value,
    )
    group_in, group_codes, group_gates = (
        lax.all_gather(hidden_b, "seq", axis=0, tiled=True),
        lax.all_gather(route_rows.astype(bf16), "seq", axis=0, tiled=True),
        lax.all_gather(picked.astype(bf16), "seq", axis=0, tiled=True),
    )
    pair_ids, valid = group_slots(group_codes.reshape(-1).astype(jnp.int32), capacity, EXPERTS)
    token_ids = pair_ids // 2
    slot_gates = jnp.where(valid, group_gates.reshape(-1)[pair_ids].astype(f32), 0.0)
    expert_in = group_in[token_ids]
    w_gate = expert_blocks[:, 0]
    w_up = expert_blocks[:, 1]
    w_down = expert_blocks[:, 2]
    gate_act = jnp.einsum("ecd,ejdn->ecjn", expert_in, w_gate, preferred_element_type=f32)
    up_act = jnp.einsum("ecd,ejdn->ecjn", expert_in, w_up, preferred_element_type=f32)
    act_b = (jax.nn.silu(gate_act) * up_act).astype(bf16)
    expert_out = jnp.einsum("ecjn,ejdn->ecd", act_b, w_down, preferred_element_type=f32)
    partial_out = (
        jnp.zeros((group_rows, D), f32)
        .at[token_ids.reshape(-1)]
        .add((expert_out * slot_gates[..., None]).reshape(-1, D))
    )
    moe_rows = lax.psum_scatter(
        partial_out.astype(jnp.bfloat16), "seq", scatter_dimension=0, tiled=True
    ).astype(jnp.float32)
    block_rows = mid_rows + moe_rows + local_out
    grad_b = cotangent[0]
    grad_rows = grad_b.astype(f32)
    group_grad = lax.all_gather(grad_b, "seq", axis=0, tiled=True)
    slot_grad = group_grad[token_ids].astype(f32)
    out_grad_b = (slot_grad * slot_gates[..., None]).astype(bf16)
    gate_grad_slots = jnp.where(valid, jnp.sum(slot_grad * expert_out, axis=-1), 0.0)
    act_grad = jnp.einsum("ecd,ejdn->ecjn", out_grad_b, w_down, preferred_element_type=f32)
    sigmoid_gate = jax.nn.sigmoid(gate_act)
    gate_grad_b = (
        act_grad * up_act * sigmoid_gate * (1.0 + gate_act * (1.0 - sigmoid_gate))
    ).astype(bf16)
    up_grad_b = (act_grad * gate_act * sigmoid_gate).astype(bf16)
    down_w_grad = jnp.einsum("ecjn,ecd->ejdn", act_b, out_grad_b, preferred_element_type=f32)
    gate_w_grad = jnp.einsum("ecd,ecjn->ejdn", expert_in, gate_grad_b, preferred_element_type=f32)
    up_w_grad = jnp.einsum("ecd,ecjn->ejdn", expert_in, up_grad_b, preferred_element_type=f32)
    in_grad = jnp.einsum(
        "ecjn,ejdn->ecd", gate_grad_b, w_gate, preferred_element_type=f32
    ) + jnp.einsum("ecjn,ejdn->ecd", up_grad_b, w_up, preferred_element_type=f32)

    expert_grads = (
        jnp.stack([gate_w_grad, up_w_grad, down_w_grad], axis=1)
        .reshape(-1, D, BW)
        .astype(bf16)
    )
    target = ring_arr[:, None] * n_local + jnp.arange(n_local, dtype=jnp.int32)[None, :]
    place = (owner_row[attn_row:][None, None, :] == target[:, :, None]).astype(bf16)
    slotted = jnp.einsum(
        "qib,brc->qirc", place, expert_grads, preferred_element_type=bf16
    )
    red_a, red_b = ring_reduce_scatter(
        slotted[:, :, : D // 2], slotted[:, :, D // 2 :], dp_ring, "dp"
    )
    expert_owned = jnp.concatenate([red_a, red_b], axis=1)

    token_grad = (
        jnp.zeros((group_rows, D), f32).at[token_ids.reshape(-1)].add(in_grad.reshape(-1, D))
    )
    pair_grad = (
        jnp.zeros((2 * group_rows,), f32)
        .at[pair_ids.reshape(-1)]
        .add(gate_grad_slots.reshape(-1))
        .reshape(group_rows, 2)
    )
    moe_grad, picked_grad = (
        lax.psum_scatter(
            token_grad.astype(jnp.bfloat16), "seq", scatter_dimension=0, tiled=True
        ).astype(jnp.float32),
        lax.psum_scatter(
            pair_grad.astype(jnp.bfloat16), "seq", scatter_dimension=0, tiled=True
        ).astype(jnp.float32),
    )
    hidden_local, prior_grad, router_grad, router_prior_grad, mix_grad, value_grad_small = (
        local_back((grad_rows, picked_grad))
    )
    hidden_grad = hidden_local + moe_grad
    _, second_norm_back = jax.vjp(rms_scale, mid_rows, gain_moe)
    mid_norm_grad, gain_moe_grad = second_norm_back(hidden_grad)
    mid_grad = grad_rows + mid_norm_grad
    attn_grad_b = mid_grad.astype(bf16)
    out_w_grad = jnp.dot(context_b.T, attn_grad_b, preferred_element_type=f32)
    context_grad_b = jnp.dot(attn_grad_b, weight_out.T, preferred_element_type=f32).astype(bf16)
    context_grad_heads = context_grad_b.reshape(tok_rows, HEADS, HEAD)
    delta = jnp.einsum("qhd,hqd->hq", context_grad_heads.astype(f32), context)

    def make_backward():

        def backward_block(carry, key_block, value_block, offset):

            def backward_visit(inner):
                query_grad = inner[0]
                count = key_block.shape[0]
                key_heads = key_block.reshape(count, HEADS, HEAD)
                value_heads = value_block.reshape(count, HEADS, HEAD)
                scores = (
                    jnp.einsum("qhd,khd->hqk", queries, key_heads, preferred_element_type=f32)
                    * score_scale
                )
                allowed = (offset + jnp.arange(count, dtype=jnp.int32))[None, :] <= positions[
                    :, None
                ]
                probs = jnp.where(allowed[None], jnp.exp(scores - log_total[..., None]), 0.0)
                prob_grad = jnp.einsum(
                    "qhd,khd->hqk", context_grad_heads, value_heads, preferred_element_type=f32
                )
                score_grad_b = (probs * (prob_grad - delta[..., None])).astype(bf16)
                query_grad = (
                    query_grad
                    + jnp.einsum(
                        "hqk,khd->qhd", score_grad_b, key_heads, preferred_element_type=f32
                    )
                    * score_scale
                )
                value_part = jnp.einsum(
                    "hqk,qhd->khd",
                    probs.astype(bf16),
                    context_grad_heads,
                    preferred_element_type=f32,
                )
                key_part = (
                    jnp.einsum("hqk,qhd->khd", score_grad_b, queries, preferred_element_type=f32)
                    * score_scale
                )
                key_grads = add_rows(inner[1], key_part.reshape(count, D), offset)
                value_grads = add_rows(inner[2], value_part.reshape(count, D), offset)
                return (query_grad, key_grads, value_grads)

            return lax.cond(offset <= last_query, backward_visit, lambda inner: inner, carry)

        def backward_piece(carry, piece, start):
            return over_blocks(carry, piece[0], piece[1], tok_rows, backward_block)

        return backward_piece

    query_zero = jnp.zeros((tok_rows, HEADS, HEAD), f32)
    back_fn = make_backward()
    back_init = (query_zero, jnp.zeros((group_rows, D), f32), jnp.zeros((group_rows, D), f32))
    folded = back_fn(back_init, piece, jnp.int32(0))
    query_grad = folded[0]
    key_grad, value_grad = (
        lax.psum_scatter(
            folded[1].astype(jnp.bfloat16), "seq", scatter_dimension=0, tiled=True
        ).astype(jnp.float32),
        lax.psum_scatter(
            folded[2].astype(jnp.bfloat16), "seq", scatter_dimension=0, tiled=True
        ).astype(jnp.float32),
    )
    query_rot = rotate(query_grad, -positions).reshape(tok_rows, D)
    key_rot = rotate(key_grad.reshape(tok_rows, HEADS, HEAD), -positions).reshape(tok_rows, D)
    proj_grad_b = jnp.concatenate([query_rot, key_rot, value_grad], axis=1).astype(bf16)
    qkv_w_grad = jnp.dot(normed_b.T, proj_grad_b, preferred_element_type=f32)
    normed_grad = jnp.dot(proj_grad_b, weight_qkv.T, preferred_element_type=f32)
    _, first_norm_back = jax.vjp(rms_scale, x_rows, gain_attn)
    x_norm_grad, gain_attn_grad = first_norm_back(normed_grad)
    input_grad = mid_grad + x_norm_grad
    attn_w_grad = jnp.concatenate([qkv_w_grad, out_w_grad], axis=1)
    attn_cols = lax.psum_scatter(
        attn_w_grad.astype(jnp.bfloat16), "seq", scatter_dimension=1, tiled=True
    ).astype(jnp.float32)
    attn_blocks = attn_cols.reshape(D, attn_row, BW).transpose(1, 0, 2)
    attn_sum = lax.psum(attn_blocks.astype(bf16), "dp")
    owned_grad = expert_owned + jnp.einsum(
        "bi,brc->irc", attn_sel, attn_sum, preferred_element_type=f32
    )
    new_masters, new_left, new_right = shampoo_update(
        masters, owned_grad, stat_left, stat_right, root_left, root_right
    )
    small_local = pack_small(
        gain_attn_grad, gain_moe_grad, router_grad, router_prior_grad, mix_grad, value_grad_small
    )
    small_size = small_local.shape[0]
    n_dev = seq_count * dp_count
    small_pad = (-small_size) % n_dev
    small_part = lax.psum_scatter(
        jnp.pad(small_local, (0, small_pad)), ("seq", "dp"), scatter_dimension=0, tiled=True
    )
    small_total = lax.all_gather(small_part, ("seq", "dp"), axis=0, tiled=True)[:small_size]
    small_now = pack_small(gain_attn, gain_moe, router, router_prior, const_mix, const_value)
    new_small, new_first, new_second = adam_update(small_now, small_total, adam_first, adam_second)
    return (
        block_rows.astype(bf16)[None],
        input_grad[None],
        prior_grad[None],
        owned_grad,
        new_masters,
        new_left,
        new_right,
        small_total,
        new_small,
        new_first,
        new_second,
    )


def solution(mesh):
    in_specs = (
        P("dp", "seq", None),
        P("dp", "seq", None),
        P("dp", "seq", None),
        P("dp", "seq", None),
        P(("seq", "dp"), None, None),
        P("seq", None),
        P(("seq", "dp"), None, None),
        P(("seq", "dp"), None, None),
        P(("seq", "dp"), None, None),
        P(("seq", "dp"), None, None),
        P(),
        P(),
        P(),
        P(),
        P(),
        P(),
        P(),
        P(),
    )
    out_specs = (
        P("dp", "seq", None),
        P("dp", "seq", None),
        P("dp", "seq", None),
        P(("seq", "dp"), None, None),
        P(("seq", "dp"), None, None),
        P(("seq", "dp"), None, None),
        P(("seq", "dp"), None, None),
        P(),
        P(),
        P(),
        P(),
    )
    return jax.shard_map(partial(body, snake_ring(mesh, "dp")), mesh=mesh, in_specs=in_specs, out_specs=out_specs, check_vma=False)
```
